512 devices in a mesh: seq: 64 (over x, z), mp: 8 (over y, core).
Axes of the slice: x: 4, y: 4, z: 16, core: 2. Of those that a mesh axis runs over, the one named last changes fastest.
Arguments:
- hidden: bfloat16 [8192, 4096], P('seq'), may hold values from -6 to 6
- cache_keys: bfloat16 [8192, 1024], P('seq', 'mp'), may hold values from -1000 to 1000
- cache_values: bfloat16 [8192, 1024], P('seq', 'mp'), may hold values from -6 to 6
- query_weight: bfloat16 [4096, 4096], P('seq', 'mp'), may hold values from -0.09375 to 0.09375
- key_weight: bfloat16 [4096, 1024], P('seq', 'mp'), may hold values from -0.09375 to 0.09375
- value_weight: bfloat16 [4096, 1024], P('seq', 'mp'), may hold values from -0.09375 to 0.09375
- out_weight: bfloat16 [4096, 4096], P('seq', 'mp'), may hold values from -0.09375 to 0.09375
- decode_input: bfloat16 [9, 4096], replicated, may hold values from -6 to 6
- lengths: int32 [9], replicated, may hold values from 1 to 4096, as said below
- prefix: int32 [9], replicated, may hold values from 0 to 3276, as said below
Outputs:
- layer_out: bfloat16 [8192, 4096], P('seq', 'mp')
- decode_out: bfloat16 [9, 4096], P(None, 'mp')
The draws below stay inside these ranges and needn't reach their ends.
Inputs may be any that keep to these rules, and one draw needn't show every extreme that they name: The lengths sum to 8192; one request holds exactly half of the slots. Each request has at least one slot after its cached prefix; the request that holds half of the slots has a cached prefix of exactly 3276; some other request has none.
All inputs are finite; a program needn't handle non-finite values.
Results may differ from the reference program's by a relative error of at most 0.012.
Values may be sent and summed in bfloat16 or wider, within the bound.
No kernel may reach another device: no remote copies, remote signals or barrier semaphores. Data moves between devices by JAX's collectives and lax.ppermute only.
A program may use at most 64 MiB of HBM per device.

```python
import math
import jax
import jax.numpy as jnp
from jax import lax

D = 4096
HEADS = 32
KV_HEADS = 8
HEAD = 128
WINDOW = 4096
REQS = 9
CTX = 8192


def request_lengths(key):
    longest = CTX // 2
    remaining = CTX - longest
    picked = jax.random.permutation(jax.random.fold_in(key, 11), remaining - 1)[:REQS - 2] + 1
    cut_points = jnp.sort(picked.astype(jnp.int32))
    bounds = jnp.concatenate([jnp.zeros((1,), jnp.int32), cut_points, jnp.full((1,), remaining, jnp.int32)])
    shorter = bounds[1:] - bounds[:-1]
    every_length = jnp.concatenate([jnp.full((1,), longest, jnp.int32), shorter])
    shuffled = jax.random.permutation(jax.random.fold_in(key, 12), REQS)
    return every_length[shuffled]


def draw_lengths(key, part):
    return request_lengths(key)


def draw_prefix(key, part):
    request_sizes = request_lengths(key)
    share = jax.random.randint(jax.random.fold_in(key, 13), (REQS,), 30, 81).astype(jnp.int32)
    base_prefix = jnp.minimum(request_sizes * share // 100, request_sizes - 1).astype(jnp.int32)
    is_long = request_sizes == CTX // 2
    request_ids = jnp.arange(REQS, dtype=jnp.int32)
    long_index = jnp.sum(jnp.where(is_long, request_ids, 0)).astype(jnp.int32)
    empty_index = (long_index + 1) % REQS
    with_empty = jnp.where(request_ids == empty_index, 0, base_prefix).astype(jnp.int32)
    return jnp.where(is_long, CTX * 2 // 5, with_empty).astype(jnp.int32)


def draw_cache_keys(key, part):
    base_keys = jax.random.normal(jax.random.fold_in(key, 21), (CTX, KV_HEADS * HEAD), jnp.float32)
    base_keys = jnp.clip(base_keys, -6.0, 6.0)
    return base_keys.astype(jnp.bfloat16)


def level_of(rng, shape, split, smallest, high):
    factor_of, own = 1.0, jax.random.fold_in(rng, 6)
    for axis_at, parts in split:
        heights = jnp.exp(jax.random.uniform(jax.random.fold_in(own, axis_at), (parts,), jnp.float32, smallest / len(split), high / len(split)))
        factor_of = factor_of * jnp.repeat(heights, shape[axis_at] // parts).reshape([-1 if axis == axis_at else 1 for axis in range(len(shape))])
    return factor_of


def normal_values(stream_key, dims, scale, limit, shards=(), held_as=jnp.bfloat16):
    gain = level_of(stream_key, dims, shards, -0.22, 0.18) if shards else 1.0
    drawn = jax.random.normal(stream_key, dims, jnp.float32) * scale * gain
    return jnp.minimum(jnp.maximum(drawn, -limit), limit).astype(held_as)


def setup_inputs(seed: int = 0) -> dict:
    key_list = jax.random.split(jax.random.key(seed), 11)
    hidden = normal_values(key_list[0], (CTX, D), 1.0, 6.0, ((0, 64),))
    cache_keys = draw_cache_keys(jax.random.fold_in(key_list[10], 71), 0)
    cache_values = normal_values(key_list[2], (CTX, KV_HEADS * HEAD), 1.0, 6.0, ((0, 64), (1, 8)))
    query_weight = normal_values(key_list[3], (D, HEADS * HEAD), D ** -0.5, 0.09375, ((0, 64), (1, 8)))
    key_weight = normal_values(key_list[4], (D, KV_HEADS * HEAD), D ** -0.5, 0.09375, ((0, 64), (1, 8)))
    value_weight = normal_values(key_list[5], (D, KV_HEADS * HEAD), D ** -0.5, 0.09375, ((0, 64), (1, 8)))
    out_weight = normal_values(key_list[6], (HEADS * HEAD, D), (HEADS * HEAD) ** -0.5, 0.09375, ((0, 64), (1, 8)))
    decode_input = normal_values(key_list[7], (REQS, D), 1.0, 6.0)
    lengths = draw_lengths(jax.random.fold_in(key_list[10], 71), 0)
    prefix = draw_prefix(jax.random.fold_in(key_list[10], 71), 0)
    return {"hidden": hidden, "cache_keys": cache_keys, "cache_values": cache_values, "query_weight": query_weight, "key_weight": key_weight, "value_weight": value_weight, "out_weight": out_weight, "decode_input": decode_input, "lengths": lengths, "prefix": prefix}


def request_of(lengths, slot_ids):
    req_ends = jnp.cumsum(lengths).astype(jnp.int32)
    return jnp.sum((slot_ids[:, None] >= req_ends[None, :]).astype(jnp.int32), axis=1).astype(jnp.int32)


def slot_table(lengths, prefix, slot_ids):
    req_ends = jnp.cumsum(lengths).astype(jnp.int32)
    req_starts = req_ends - lengths
    req_ids = request_of(lengths, slot_ids)
    matches = req_ids[:, None] == jnp.arange(lengths.shape[0], dtype=jnp.int32)[None, :]
    first_slot = jnp.sum(jnp.where(matches, req_starts[None, :], 0), axis=1).astype(jnp.int32)
    cached = jnp.sum(jnp.where(matches, prefix[None, :], 0), axis=1).astype(jnp.int32)
    positions = slot_ids - first_slot
    return req_ids, positions, positions >= cached


def rotate(matrix, positions):
    row_count = matrix.shape[0]
    head_count = matrix.shape[1] // HEAD
    half_size = HEAD // 2
    frequency = 1.0 / (10000.0 ** (jnp.arange(half_size, dtype=jnp.float32) * (2.0 / HEAD)))
    angles = positions.astype(jnp.float32)[:, None] * frequency[None, :]
    cosine = jnp.cos(angles)[:, None, :]
    sine_table = jnp.sin(angles)[:, None, :]
    shaped = matrix.reshape(row_count, head_count, HEAD)
    lower_half = shaped[:, :, :half_size]
    upper_half = shaped[:, :, half_size:]
    turned = jnp.concatenate([lower_half * cosine - upper_half * sine_table, upper_half * cosine + lower_half * sine_table], axis=-1)
    return turned.reshape(row_count, head_count * HEAD)


def attention_rows(query_grid, q_owner, q_slots, key_grid, value_grid, k_owner, k_slots):
    scores = jnp.einsum("qcgd,kcd->cgqk", query_grid.astype(jnp.float32), key_grid.astype(jnp.float32)) * (HEAD ** -0.5)
    distance = q_slots[:, None] - k_slots[None, :]
    allowed = (q_owner[:, None] == k_owner[None, :]) & (k_slots[None, :] >= 0) & (distance >= 0) & (distance < WINDOW)
    scores = jnp.where(allowed[None, None], scores, -jnp.inf)
    peak_value = jnp.max(scores, axis=-1, keepdims=True)
    expo = jnp.exp(scores - peak_value)
    weight_sum = jnp.sum(expo, axis=-1)
    rounded = lax.optimization_barrier(expo.astype(jnp.bfloat16)).astype(jnp.float32)
    mixed = jnp.einsum("cgqk,kcd->qcgd", rounded, value_grid.astype(jnp.float32))
    return mixed / jnp.transpose(weight_sum, (2, 0, 1))[..., None]


def reference(hidden, cache_keys, cache_values, query_weight, key_weight, value_weight, out_weight, decode_input, lengths, prefix):
    group = HEADS // KV_HEADS
    slot_ids = jnp.arange(CTX, dtype=jnp.int32)
    req_ids, positions, is_new = slot_table(lengths, prefix, slot_ids)
    queries = rotate(jnp.dot(hidden, query_weight, preferred_element_type=jnp.float32), positions).astype(jnp.bfloat16)
    new_keys = rotate(jnp.dot(hidden, key_weight, preferred_element_type=jnp.float32), positions).astype(jnp.bfloat16)
    new_values = jnp.dot(hidden, value_weight, preferred_element_type=jnp.float32).astype(jnp.bfloat16)
    key_rows = jnp.where(is_new[:, None], new_keys, cache_keys)
    value_rows = jnp.where(is_new[:, None], new_values, cache_values)
    padded_keys = jnp.concatenate([jnp.zeros((WINDOW, KV_HEADS * HEAD), jnp.bfloat16), key_rows], axis=0)
    padded_values = jnp.concatenate([jnp.zeros((WINDOW, KV_HEADS * HEAD), jnp.bfloat16), value_rows], axis=0)
    padded_req = jnp.concatenate([jnp.zeros((WINDOW,), jnp.int32), req_ids], axis=0)
    span = math.gcd(512, CTX)

    def one_block(start_slot):
        query_grid = lax.dynamic_slice_in_dim(queries, start_slot, span, 0).reshape(span, KV_HEADS, group, HEAD)
        key_grid = lax.dynamic_slice_in_dim(padded_keys, start_slot, WINDOW + span, 0).reshape(WINDOW + span, KV_HEADS, HEAD)
        value_grid = lax.dynamic_slice_in_dim(padded_values, start_slot, WINDOW + span, 0).reshape(WINDOW + span, KV_HEADS, HEAD)
        q_owner = lax.dynamic_slice_in_dim(req_ids, start_slot, span, 0)
        k_owner = lax.dynamic_slice_in_dim(padded_req, start_slot, WINDOW + span, 0)
        q_slots = start_slot + jnp.arange(span, dtype=jnp.int32)
        k_slots = start_slot - WINDOW + jnp.arange(WINDOW + span, dtype=jnp.int32)
        return attention_rows(query_grid, q_owner, q_slots, key_grid, value_grid, k_owner, k_slots)

    block_starts = jnp.arange(CTX // span, dtype=jnp.int32) * span
    attn = lax.map(one_block, block_starts).reshape(CTX, HEADS * HEAD)
    attn = jnp.where(is_new[:, None], attn, 0.0).astype(jnp.bfloat16)
    layer_out = jnp.dot(attn, out_weight, preferred_element_type=jnp.float32).astype(jnp.bfloat16)

    req_ends = jnp.cumsum(lengths).astype(jnp.int32)
    decode_queries = rotate(jnp.dot(decode_input, query_weight, preferred_element_type=jnp.float32), lengths).astype(jnp.bfloat16)
    decode_keys = rotate(jnp.dot(decode_input, key_weight, preferred_element_type=jnp.float32), lengths).astype(jnp.bfloat16)
    decode_values = jnp.dot(decode_input, value_weight, preferred_element_type=jnp.float32).astype(jnp.bfloat16)

    def one_request(request):
        end_slot = req_ends[request]
        key_block = jnp.concatenate([lax.dynamic_slice_in_dim(padded_keys, end_slot, WINDOW, 0), lax.dynamic_slice_in_dim(decode_keys, request, 1, 0)], axis=0)
        value_block = jnp.concatenate([lax.dynamic_slice_in_dim(padded_values, end_slot, WINDOW, 0), lax.dynamic_slice_in_dim(decode_values, request, 1, 0)], axis=0)
        k_owner = jnp.concatenate([lax.dynamic_slice_in_dim(padded_req, end_slot, WINDOW, 0), jnp.full((1,), request, jnp.int32)], axis=0)
        k_slots = jnp.concatenate([end_slot - WINDOW + jnp.arange(WINDOW, dtype=jnp.int32), jnp.full((1,), end_slot, jnp.int32)], axis=0)
        query_grid = lax.dynamic_slice_in_dim(decode_queries, request, 1, 0).reshape(1, KV_HEADS, group, HEAD)
        return attention_rows(query_grid, jnp.full((1,), request, jnp.int32), jnp.full((1,), end_slot, jnp.int32), key_block.reshape(WINDOW + 1, KV_HEADS, HEAD), value_block.reshape(WINDOW + 1, KV_HEADS, HEAD), k_owner, k_slots)

    decode_attn = lax.map(one_request, jnp.arange(REQS, dtype=jnp.int32)).reshape(REQS, HEADS * HEAD).astype(jnp.bfloat16)
    decode_out = jnp.dot(decode_attn, out_weight, preferred_element_type=jnp.float32).astype(jnp.bfloat16)
    return layer_out, decode_out
```

```python
import jax
import jax.numpy as jnp
from jax import lax
from jax.sharding import Mesh
from jax.sharding import PartitionSpec as P

HEAD = 128
WINDOW = 4096
SEQ = ("sx", "sz")


def gather_seq(block):
    inner = lax.all_gather(block, "sz", axis=0, tiled=True)
    return lax.all_gather(inner, "sx", axis=0, tiled=True)


def request_of(lengths, slot_ids):
    req_ends = jnp.cumsum(lengths)
    return jnp.sum((slot_ids[:, None] >= req_ends[None, :]).astype(jnp.int32), axis=1)


def slot_table(lengths, prefix, slot_ids):
    req_ends = jnp.cumsum(lengths)
    req_starts = req_ends - lengths
    req_ids = request_of(lengths, slot_ids)
    matches = req_ids[:, None] == jnp.arange(lengths.shape[0], dtype=jnp.int32)[None, :]
    first_slot = jnp.sum(jnp.where(matches, req_starts[None, :], 0), axis=1)
    cached = jnp.sum(jnp.where(matches, prefix[None, :], 0), axis=1)
    positions = slot_ids - first_slot
    return (req_ids, positions, positions >= cached)


def rotate(matrix, positions):
    row_count = matrix.shape[0]
    head_count = matrix.shape[1] // HEAD
    half_size = HEAD // 2
    frequency = 1.0 / 10000.0 ** (jnp.arange(half_size, dtype=jnp.float32) * (2.0 / HEAD))
    angles = positions.astype(jnp.float32)[:, None] * frequency[None, :]
    cosine = jnp.cos(angles)[:, None, :]
    sine_table = jnp.sin(angles)[:, None, :]
    shaped = matrix.reshape(row_count, head_count, HEAD)
    lower_half = shaped[:, :, :half_size]
    upper_half = shaped[:, :, half_size:]
    turned = jnp.concatenate(
        [
            lower_half * cosine - upper_half * sine_table,
            upper_half * cosine + lower_half * sine_table,
        ],
        axis=-1,
    )
    return turned.reshape(row_count, head_count * HEAD)


def softmax_mix(scores, allowed, value_grid):
    scores = jnp.where(allowed[None, None], scores, -jnp.inf)
    peak = jnp.max(scores, axis=-1, keepdims=True)
    expo = jnp.exp(scores - peak)
    weight_sum = jnp.sum(expo, axis=-1)
    mixed = jnp.einsum(
        "cgqk,kcd->qcgd", expo.astype(jnp.bfloat16), value_grid, preferred_element_type=jnp.float32
    )
    return mixed, weight_sum


def per_device(
    hidden,
    cache_keys,
    cache_values,
    query_weight,
    key_weight,
    value_weight,
    out_weight,
    decode_input,
    lengths,
    prefix,
):
    seq_index = lax.axis_index("sx") * lax.axis_size("sz") + lax.axis_index("sz")
    slot_rows = hidden.shape[0]
    q_columns = query_weight.shape[1]
    kv_columns = key_weight.shape[1]
    kv_heads = kv_columns // HEAD
    group = q_columns // kv_columns
    request_count = lengths.shape[0]
    scale = HEAD ** (-0.5)

    weights = gather_seq(
        jnp.concatenate([query_weight, key_weight, value_weight, out_weight], axis=1)
    )
    qkv_weight = weights[:, : q_columns + 2 * kv_columns]
    out_full = weights[:, q_columns + 2 * kv_columns :]

    slot_ids = seq_index * slot_rows + jnp.arange(slot_rows, dtype=jnp.int32)
    req_ids, positions, is_new = slot_table(lengths, prefix, slot_ids)
    req_ends = jnp.cumsum(lengths)
    request_ids = jnp.arange(request_count, dtype=jnp.int32)

    stacked = jnp.concatenate([hidden, decode_input], axis=0)
    all_rows = slot_rows + request_count
    projected = jnp.dot(stacked, qkv_weight, preferred_element_type=jnp.float32)
    all_positions = jnp.concatenate([positions, lengths], axis=0)
    queries = rotate(projected[:, :q_columns], all_positions).astype(jnp.bfloat16)
    new_keys = rotate(projected[:, q_columns : q_columns + kv_columns], all_positions).astype(
        jnp.bfloat16
    )
    new_values = projected[:, q_columns + kv_columns :].astype(jnp.bfloat16)

    local_keys = jnp.where(is_new[:, None], new_keys[:slot_rows], cache_keys)
    local_values = jnp.where(is_new[:, None], new_values[:slot_rows], cache_values)
    kv_all = gather_seq(jnp.concatenate([local_keys, local_values], axis=1))
    total_slots = kv_all.shape[0]
    key_all = kv_all[:, :kv_columns].reshape(total_slots, kv_heads, HEAD)
    value_all = kv_all[:, kv_columns:].reshape(total_slots, kv_heads, HEAD)

    query_grid = queries.reshape(all_rows, kv_heads, group, HEAD)

    reach = WINDOW + slot_rows
    padded = jnp.concatenate([jnp.zeros((WINDOW, 2 * kv_columns), kv_all.dtype), kv_all], axis=0)
    window_kv = lax.dynamic_slice_in_dim(padded, seq_index * slot_rows, reach, 0)
    window_keys = window_kv[:, :kv_columns].reshape(reach, kv_heads, HEAD)
    window_values = window_kv[:, kv_columns:].reshape(reach, kv_heads, HEAD)
    k_slots = seq_index * slot_rows - WINDOW + jnp.arange(reach, dtype=jnp.int32)
    k_owner = request_of(lengths, k_slots)
    active_grid = query_grid[:slot_rows]
    scores = (
        jnp.einsum("qcgd,kcd->cgqk", active_grid, window_keys, preferred_element_type=jnp.float32)
        * scale
    )
    distance = slot_ids[:, None] - k_slots[None, :]
    allowed = (
        (req_ids[:, None] == k_owner[None, :])
        & (k_slots[None, :] >= 0)
        & (distance >= 0)
        & (distance < WINDOW)
    )
    mixed, weight_sum = softmax_mix(scores, allowed, window_values)
    prefill = mixed / jnp.transpose(weight_sum, (2, 0, 1))[..., None]
    prefill_attn = jnp.where(
        is_new[:, None], prefill.reshape(slot_rows, q_columns), 0.0
    ).astype(jnp.bfloat16)

    decode_grid = query_grid[slot_rows:]
    own_keys = new_keys[slot_rows:].reshape(request_count, kv_heads, HEAD)
    own_values = new_values[slot_rows:].reshape(request_count, kv_heads, HEAD)
    all_slots = jnp.arange(total_slots, dtype=jnp.int32)
    all_owner = request_of(lengths, all_slots)
    context_scores = (
        jnp.einsum("qcgd,kcd->cgqk", decode_grid, key_all, preferred_element_type=jnp.float32)
        * scale
    )
    own_scores = (
        jnp.einsum("qcgd,qcd->cgq", decode_grid, own_keys, preferred_element_type=jnp.float32)
        * scale
    )
    d_distance = req_ends[:, None] - all_slots[None, :]
    d_allowed = (
        (request_ids[:, None] == all_owner[None, :]) & (d_distance >= 0) & (d_distance < WINDOW)
    )
    context_scores = jnp.where(d_allowed[None, None], context_scores, -jnp.inf)
    peak = jnp.maximum(jnp.max(context_scores, axis=-1), own_scores)
    context_expo = jnp.exp(context_scores - peak[..., None])
    own_expo = jnp.exp(own_scores - peak)
    d_sum = jnp.sum(context_expo, axis=-1) + own_expo
    d_mixed = jnp.einsum(
        "cgqk,kcd->qcgd",
        context_expo.astype(jnp.bfloat16),
        value_all,
        preferred_element_type=jnp.float32,
    )
    own_weight = jnp.transpose(own_expo.astype(jnp.bfloat16).astype(jnp.float32), (2, 0, 1))
    d_mixed = d_mixed + own_weight[..., None] * own_values.astype(jnp.float32)[:, :, None, :]
    decode_attn = (d_mixed / jnp.transpose(d_sum, (2, 0, 1))[..., None]).reshape(
        request_count, q_columns
    ).astype(jnp.bfloat16)

    local_heads = jnp.concatenate([prefill_attn, decode_attn], axis=0)
    all_heads = lax.all_gather(local_heads, "mp", axis=1, tiled=True)
    out = jnp.dot(all_heads, out_full, preferred_element_type=jnp.float32).astype(jnp.bfloat16)
    return (out[:slot_rows], out[slot_rows:])


def solution(mesh):
    seq_size, mp_size = mesh.devices.shape
    inner = 16 if seq_size % 16 == 0 else seq_size
    grid = Mesh(mesh.devices.reshape(seq_size // inner, inner, mp_size), ("sx", "sz", "mp"))
    return jax.shard_map(
        per_device,
        mesh=grid,
        in_specs=(
            P(SEQ, None),
            P(SEQ, "mp"),
            P(SEQ, "mp"),
            P(SEQ, "mp"),
            P(SEQ, "mp"),
            P(SEQ, "mp"),
            P(SEQ, "mp"),
            P(),
            P(),
            P(),
        ),
        out_specs=(P(SEQ, "mp"), P(None, "mp")),
        check_vma=False,
    )
```
